1024 devices in a mesh: gx: 4 (over y), gy: 8 (over x, core), gz: 32 (over z).
Axes of the slice: x: 4, y: 4, z: 32, core: 2. Of those that a mesh axis runs over, the one named last changes fastest.
Arguments:
- element_load: float32 [160, 136, 512], P('gz', 'gy', 'gx'), may hold values from -6 to 6
- conductivity: float32 [64, 64, 256], P('gz', 'gy', 'gx'), may hold values from 0.2 to 5
Outputs:
- corrected: float32 [160, 136, 512], P('gz', 'gy', 'gx')
The draws below stay inside these ranges and needn't reach their ends.
All inputs are finite; a program needn't handle non-finite values.
Results may differ from the reference program's by a relative error of at most 0.00002.
Values sent between devices are 32-bit elements; how exact they have to be, the bound alone decides.
No kernel may reach another device: no remote copies, remote signals or barrier semaphores. Data moves between devices by JAX's collectives and lax.ppermute only.
A program may use at most 32 MiB of HBM per device.

```python
import math
import jax
import jax.numpy as jnp
import numpy as np
from jax import lax

DEG1 = 3
DEG2 = 4
NODES_Z = 160
NODES_Y = 136
NODES_X = 512
CELLS_Z = 64
CELLS_Y = 64
CELLS_X = 256
N_GX = 4
N_GY = 8
N_GZ = 32


def levels(rng, dims, split, low, top_value):
    gain, own = 1.0, jax.random.fold_in(rng, 6)
    for axis_at, blocks in split:
        steps = jnp.exp(jax.random.uniform(jax.random.fold_in(own, axis_at), (blocks,), jnp.float32, low / len(split), top_value / len(split)))
        gain = gain * jnp.repeat(steps, dims[axis_at] // blocks).reshape([-1 if axis == axis_at else 1 for axis in range(len(dims))])
    return gain


def noise(stream_key, shape, scale, reach, cuts=(), kind=jnp.bfloat16):
    loudness = levels(stream_key, shape, cuts, -0.22, 0.18) if cuts else 1.0
    values = jax.random.normal(stream_key, shape, jnp.float32) * scale * loudness
    return jnp.minimum(jnp.maximum(values, -reach), reach).astype(kind)


def setup_inputs(seed: int = 0) -> dict:
    key_of = jax.random.split(jax.random.key(seed), 3)
    return {
        "element_load": noise(key_of[0], (NODES_Z, NODES_Y, NODES_X), 1.0, 6.0, ((0, 32), (1, 8), (2, 4)), jnp.float32),
        "conductivity": jnp.clip(jnp.exp(math.log(5.0) - 3.218876 * jax.random.uniform(key_of[1], (CELLS_Z, CELLS_Y, CELLS_X), jnp.float32) ** levels(key_of[1], (CELLS_Z, CELLS_Y, CELLS_X), ((0, 32), (1, 8), (2, 4)), -0.2, 0.2)), 0.2, 5.0),
    }


reaction_rate = 0.05
lower_bound = 0.25
upper_bound = 2.5
mass_table = [[4.0 / 30.0, 2.0 / 30.0, -1.0 / 30.0], [2.0 / 30.0, 16.0 / 30.0, 2.0 / 30.0], [-1.0 / 30.0, 2.0 / 30.0, 4.0 / 30.0]]
stiff_table = [[7.0 / 3.0, -8.0 / 3.0, 1.0 / 3.0], [-8.0 / 3.0, 16.0 / 3.0, -8.0 / 3.0], [1.0 / 3.0, -8.0 / 3.0, 7.0 / 3.0]]


def pad_axis(values, which_axis, before, after):
    widths = [(0, 0)] * values.ndim
    widths[which_axis] = (before, after)
    return jnp.pad(values, widths)


def contract(values, matrix, which_axis):
    pieces = [lax.index_in_dim(values, a, which_axis, keepdims=False) for a in range(3)]
    results = [matrix[b][0] * pieces[0] + matrix[b][1] * pieces[1] + matrix[b][2] * pieces[2] for b in range(3)]
    return jnp.stack(results, axis=which_axis)


def node_slices(node_field, which_axis, periodic):
    if periodic:
        length_here = node_field.shape[which_axis]
        even_nodes = lax.slice_in_dim(node_field, 0, length_here, 2, axis=which_axis)
        odd_nodes = lax.slice_in_dim(node_field, 1, length_here, 2, axis=which_axis)
        return [even_nodes, odd_nodes, jnp.roll(even_nodes, -1, axis=which_axis)]
    elements = (node_field.shape[which_axis] - 1) // 2
    return [lax.slice_in_dim(node_field, a, a + 2 * elements - 1, 2, axis=which_axis) for a in range(3)]


def spread(node_field, periodic):
    along_x = jnp.stack(node_slices(node_field, 2, periodic), 0)
    along_y = jnp.stack(node_slices(along_x, 2, False), 1)
    return jnp.stack(node_slices(along_y, 2, False), 2)


def fold_back(stacked, which_axis, periodic):
    lower_part = stacked[0]
    middle_part = stacked[1]
    upper_part = stacked[2]
    target = which_axis - 1
    elements = lower_part.shape[target]
    if periodic:
        even_nodes = lower_part + jnp.roll(upper_part, 1, axis=target)
    else:
        even_full = pad_axis(lower_part, target, 0, 1) + pad_axis(upper_part, target, 1, 0)
        even_nodes = lax.slice_in_dim(even_full, 0, elements, axis=target)
        tail_node = lax.slice_in_dim(even_full, elements, elements + 1, axis=target)
    woven_nodes = jnp.stack([even_nodes, middle_part], axis=target + 1)
    node_shape = list(even_nodes.shape)
    node_shape[target] = 2 * elements
    woven_nodes = woven_nodes.reshape(node_shape)
    if periodic:
        return woven_nodes
    return jnp.concatenate([woven_nodes, tail_node], axis=target)


def gather_elements(product, periodic):
    folded = fold_back(product, 5, periodic)
    folded = fold_back(folded, 3, False)
    return fold_back(folded, 1, False)


def apply_local(node_field, conduct, stiff_scale, mass_scale, periodic):
    node_values = spread(node_field, periodic)
    mass_depth = contract(node_values, mass_table, 2)
    mass_plane = contract(mass_depth, mass_table, 1)
    stiffness = contract(mass_plane, stiff_table, 0)
    mass_width = contract(node_values, mass_table, 0)
    stiffness = stiffness + contract(contract(mass_width, stiff_table, 1), mass_table, 2)
    mass_face = contract(mass_width, mass_table, 1)
    stiffness = stiffness + contract(mass_face, stiff_table, 2)
    product = (stiff_scale * conduct) * stiffness + mass_scale * contract(mass_face, mass_table, 2)
    return gather_elements(product, periodic)


def diag_tables():
    stiff_line = np.array([stiff_table[a][a] for a in range(3)])
    mass_line = np.array([mass_table[a][a] for a in range(3)])
    stiff_part = (stiff_line[:, None, None] * mass_line[None, :, None] * mass_line[None, None, :]
                  + mass_line[:, None, None] * stiff_line[None, :, None] * mass_line[None, None, :]
                  + mass_line[:, None, None] * mass_line[None, :, None] * stiff_line[None, None, :])
    mass_part = mass_line[:, None, None] * mass_line[None, :, None] * mass_line[None, None, :]
    return stiff_part.reshape(3, 3, 3, 1, 1, 1), mass_part.reshape(3, 3, 3, 1, 1, 1)


def diag_local(conduct, stiff_scale, mass_scale, periodic):
    stiff_part, mass_part = diag_tables()
    product = (stiff_scale * conduct) * jnp.asarray(stiff_part, conduct.dtype) + mass_scale * jnp.asarray(mass_part, conduct.dtype)
    return gather_elements(product, periodic)


def coarse_conduct(conduct):
    layers_z, rows_y, cols_x = conduct.shape
    shaped = conduct.reshape(layers_z // 2, 2, rows_y // 2, 2, cols_x // 2, 2)
    return jnp.sum(shaped, axis=(1, 3, 5)) * 0.125


def prolong_axis(coarse, which_axis):
    pieces = node_slices(coarse, which_axis, False)
    fine_parts = [pieces[0],
                  0.375 * pieces[0] + 0.75 * pieces[1] - 0.125 * pieces[2],
                  pieces[1],
                  -0.125 * pieces[0] + 0.75 * pieces[1] + 0.375 * pieces[2]]
    woven_nodes = jnp.stack(fine_parts, axis=which_axis + 1)
    node_shape = list(pieces[0].shape)
    node_shape[which_axis] = 4 * pieces[0].shape[which_axis]
    woven_nodes = woven_nodes.reshape(node_shape)
    length_here = coarse.shape[which_axis]
    tail_node = lax.slice_in_dim(coarse, length_here - 1, length_here, axis=which_axis)
    return jnp.concatenate([woven_nodes, tail_node], axis=which_axis)


def prolong_all(coarse):
    result = prolong_axis(coarse, 0)
    result = prolong_axis(result, 1)
    return prolong_axis(result, 2)


def restrict_axis(fine, which_axis):
    length_here = fine.shape[which_axis]
    elements = (length_here - 1) // 4
    quarters = [lax.slice_in_dim(fine, q, q + 4 * elements - 3, 4, axis=which_axis) for q in range(4)]
    coarse_parts = [quarters[0] + 0.375 * quarters[1] - 0.125 * quarters[3],
                    0.75 * quarters[1] + quarters[2] + 0.75 * quarters[3],
                    -0.125 * quarters[1] + 0.375 * quarters[3]]
    folded = fold_back(jnp.stack(coarse_parts, 0), which_axis + 1, False)
    tail_node = lax.slice_in_dim(fine, length_here - 1, length_here, axis=which_axis)
    return folded + pad_axis(tail_node, which_axis, 2 * elements, 0)


def restrict_all(fine):
    result = restrict_axis(fine, 0)
    result = restrict_axis(result, 1)
    return restrict_axis(result, 2)


def chebyshev(right_side, diagonal, operate, degree):
    centre = 0.5 * (upper_bound + lower_bound)
    half_width = 0.5 * (upper_bound - lower_bound)
    sharpness = centre / half_width
    factor = 1.0 / sharpness
    scaled = 1.0 / diagonal
    update = (scaled * right_side) * (1.0 / centre)
    solution = update
    for k in range(1, degree):
        residual = right_side - operate(solution)
        next_factor = 1.0 / (2.0 * sharpness - factor)
        update = (next_factor * factor) * update + (2.0 * next_factor / half_width) * (scaled * residual)
        solution = solution + update
        factor = next_factor
    return solution


def to_blocks(global_array, splits):
    shaped = global_array.reshape(splits[0], global_array.shape[0] // splits[0], splits[1],
                                  global_array.shape[1] // splits[1], splits[2], global_array.shape[2] // splits[2])
    return shaped.transpose(0, 2, 4, 1, 3, 5)


def from_blocks(blocks):
    sizes_all = blocks.shape
    shaped = blocks.transpose(0, 3, 1, 4, 2, 5)
    return shaped.reshape(sizes_all[0] * sizes_all[3], sizes_all[1] * sizes_all[4], sizes_all[2] * sizes_all[5])


def per_device(function, arrays):
    def one_slab(slab_arrays):
        return jax.vmap(jax.vmap(function))(slab_arrays)

    return lax.map(one_slab, arrays)


def assemble_blocks(blocks):
    for p, q in ((0, 3), (1, 4), (2, 5)):
        length_here = blocks.shape[q]
        main_part = lax.slice_in_dim(blocks, 0, length_here - 1, axis=q)
        tail_part = lax.slice_in_dim(blocks, length_here - 1, length_here, axis=q)
        first_layer = lax.slice_in_dim(main_part, 0, 1, axis=q) + jnp.roll(tail_part, 1, axis=p)
        main_part = jnp.concatenate([first_layer, lax.slice_in_dim(main_part, 1, length_here - 1, axis=q)], axis=q)
        blocks = jnp.concatenate([main_part, jnp.roll(lax.slice_in_dim(main_part, 0, 1, axis=q), -1, axis=p)], axis=q)
    return blocks


def reference(element_load, conductivity):
    splits = (N_GZ, N_GY, N_GX)
    load_blocks = pad_axis(to_blocks(element_load, splits), 5, 0, 1)
    cond_blocks = to_blocks(conductivity, splits)
    diag_blocks = per_device(lambda members: diag_local(members[0], 1.0, reaction_rate, False), (cond_blocks,))
    right_side = assemble_blocks(load_blocks)
    diagonal = assemble_blocks(diag_blocks)

    def local_fine(node_field):
        return per_device(lambda members: apply_local(members[0], members[1], 1.0, reaction_rate, False), (node_field, cond_blocks))

    def operate_fine(node_field):
        return assemble_blocks(local_fine(node_field))

    smooth = chebyshev(right_side, diagonal, operate_fine, DEG1)
    partial_value = load_blocks - local_fine(smooth)
    coarse_load = per_device(lambda members: restrict_all(members[0]), (partial_value,))
    coarse_cond = per_device(lambda members: coarse_conduct(members[0]), (cond_blocks,))
    coarse_mass = 8.0 * reaction_rate
    coarse_diag = per_device(lambda members: diag_local(members[0], 2.0, coarse_mass, False), (coarse_cond,))

    def operate_coarse(node_field):
        return assemble_blocks(per_device(lambda members: apply_local(members[0], members[1], 2.0, coarse_mass, False), (node_field, coarse_cond)))

    correction = chebyshev(assemble_blocks(coarse_load), assemble_blocks(coarse_diag), operate_coarse, DEG2)
    corrected = smooth + per_device(lambda members: prolong_all(members[0]), (correction,))
    trimmed = corrected[:, :, :, :, :, : corrected.shape[5] - 1]
    return from_blocks(trimmed)
```

```python
import jax
import jax.numpy as jnp
import numpy as np
from jax import lax
from jax.sharding import PartitionSpec as P

DEG1 = 3
DEG2 = 4


reaction_rate = 0.05
lower_bound = 0.25
upper_bound = 2.5
mass_table = [
    [4.0 / 30.0, 2.0 / 30.0, -1.0 / 30.0],
    [2.0 / 30.0, 16.0 / 30.0, 2.0 / 30.0],
    [-1.0 / 30.0, 2.0 / 30.0, 4.0 / 30.0],
]
stiff_table = [
    [7.0 / 3.0, -8.0 / 3.0, 1.0 / 3.0],
    [-8.0 / 3.0, 16.0 / 3.0, -8.0 / 3.0],
    [1.0 / 3.0, -8.0 / 3.0, 7.0 / 3.0],
]


def padded(cells, sides, width):
    for axis, dim in sides:
        count = lax.axis_size(axis)
        head = lax.slice_in_dim(cells, 0, width, axis=dim)
        tail = lax.slice_in_dim(cells, cells.shape[dim] - width, cells.shape[dim], axis=dim)
        cells = jnp.concatenate(
            [
                lax.ppermute(tail, axis, [(i, (i + 1) % count) for i in range(count)]),
                cells,
                lax.ppermute(head, axis, [((i + 1) % count, i) for i in range(count)]),
            ],
            axis=dim,
        )
    return cells


def pad_axis(values, which_axis, before, after):
    widths = [(0, 0)] * values.ndim
    widths[which_axis] = (before, after)
    return jnp.pad(values, widths)


def contract(values, matrix, which_axis):
    pieces = [lax.index_in_dim(values, a, which_axis, keepdims=False) for a in range(3)]
    results = [
        matrix[b][0] * pieces[0] + matrix[b][1] * pieces[1] + matrix[b][2] * pieces[2]
        for b in range(3)
    ]
    return jnp.stack(results, axis=which_axis)


def node_slices(node_field, which_axis):
    elements = (node_field.shape[which_axis] - 1) // 2
    return [
        lax.slice_in_dim(node_field, a, a + 2 * elements - 1, 2, axis=which_axis) for a in range(3)
    ]


def spread(node_field):
    along_x = jnp.stack(node_slices(node_field, 2), 0)
    along_y = jnp.stack(node_slices(along_x, 2), 1)
    return jnp.stack(node_slices(along_y, 2), 2)


def fold_back(stacked, which_axis):
    lower_part = stacked[0]
    middle_part = stacked[1]
    upper_part = stacked[2]
    target = which_axis - 1
    elements = lower_part.shape[target]
    even_full = pad_axis(lower_part, target, 0, 1) + pad_axis(upper_part, target, 1, 0)
    even_nodes = lax.slice_in_dim(even_full, 0, elements, axis=target)
    tail_node = lax.slice_in_dim(even_full, elements, elements + 1, axis=target)
    woven_nodes = jnp.stack([even_nodes, middle_part], axis=target + 1)
    node_shape = list(even_nodes.shape)
    node_shape[target] = 2 * elements
    woven_nodes = woven_nodes.reshape(node_shape)
    return jnp.concatenate([woven_nodes, tail_node], axis=target)


def gather_elements(product):
    folded = fold_back(product, 5)
    folded = fold_back(folded, 3)
    return fold_back(folded, 1)


def apply_local(node_field, conduct, stiff_scale, mass_scale):
    node_values = spread(node_field)
    mass_depth = contract(node_values, mass_table, 2)
    mass_plane = contract(mass_depth, mass_table, 1)
    stiffness = contract(mass_plane, stiff_table, 0)
    mass_width = contract(node_values, mass_table, 0)
    stiffness = stiffness + contract(contract(mass_width, stiff_table, 1), mass_table, 2)
    mass_face = contract(mass_width, mass_table, 1)
    stiffness = stiffness + contract(mass_face, stiff_table, 2)
    product = stiff_scale * conduct * stiffness + mass_scale * contract(mass_face, mass_table, 2)
    return gather_elements(product)


def diag_tables():
    stiff_line = np.array([stiff_table[a][a] for a in range(3)])
    mass_line = np.array([mass_table[a][a] for a in range(3)])
    stiff_part = (
        stiff_line[:, None, None] * mass_line[None, :, None] * mass_line[None, None, :]
        + mass_line[:, None, None] * stiff_line[None, :, None] * mass_line[None, None, :]
        + mass_line[:, None, None] * mass_line[None, :, None] * stiff_line[None, None, :]
    )
    mass_part = mass_line[:, None, None] * mass_line[None, :, None] * mass_line[None, None, :]
    return (stiff_part.reshape(3, 3, 3, 1, 1, 1), mass_part.reshape(3, 3, 3, 1, 1, 1))


def diag_local(conduct, stiff_scale, mass_scale):
    stiff_part, mass_part = diag_tables()
    product = stiff_scale * conduct * jnp.asarray(
        stiff_part, conduct.dtype
    ) + mass_scale * jnp.asarray(mass_part, conduct.dtype)
    return gather_elements(product)


def coarse_conduct(conduct):
    layers_z, rows_y, cols_x = conduct.shape
    shaped = conduct.reshape(layers_z // 2, 2, rows_y // 2, 2, cols_x // 2, 2)
    return jnp.sum(shaped, axis=(1, 3, 5)) * 0.125


def prolong_axis(coarse, which_axis):
    pieces = node_slices(coarse, which_axis)
    fine_parts = [
        pieces[0],
        0.375 * pieces[0] + 0.75 * pieces[1] - 0.125 * pieces[2],
        pieces[1],
        -0.125 * pieces[0] + 0.75 * pieces[1] + 0.375 * pieces[2],
    ]
    woven_nodes = jnp.stack(fine_parts, axis=which_axis + 1)
    node_shape = list(pieces[0].shape)
    node_shape[which_axis] = 4 * pieces[0].shape[which_axis]
    woven_nodes = woven_nodes.reshape(node_shape)
    length_here = coarse.shape[which_axis]
    tail_node = lax.slice_in_dim(coarse, length_here - 1, length_here, axis=which_axis)
    return jnp.concatenate([woven_nodes, tail_node], axis=which_axis)


def prolong_all(coarse):
    result = prolong_axis(coarse, 0)
    result = prolong_axis(result, 1)
    return prolong_axis(result, 2)


def restrict_axis(fine, which_axis):
    length_here = fine.shape[which_axis]
    elements = (length_here - 1) // 4
    quarters = [
        lax.slice_in_dim(fine, q, q + 4 * elements - 3, 4, axis=which_axis) for q in range(4)
    ]
    coarse_parts = [
        quarters[0] + 0.375 * quarters[1] - 0.125 * quarters[3],
        0.75 * quarters[1] + quarters[2] + 0.75 * quarters[3],
        -0.125 * quarters[1] + 0.375 * quarters[3],
    ]
    folded = fold_back(jnp.stack(coarse_parts, 0), which_axis + 1)
    tail_node = lax.slice_in_dim(fine, length_here - 1, length_here, axis=which_axis)
    return folded + pad_axis(tail_node, which_axis, 2 * elements, 0)


def restrict_all(fine):
    result = restrict_axis(fine, 0)
    result = restrict_axis(result, 1)
    return restrict_axis(result, 2)


def chebyshev(right_side, diagonal, operate, degree):
    centre = 0.5 * (upper_bound + lower_bound)
    half_width = 0.5 * (upper_bound - lower_bound)
    sharpness = centre / half_width
    factor = 1.0 / sharpness
    scaled = 1.0 / diagonal
    update = scaled * right_side * (1.0 / centre)
    solution = update
    for k in range(1, degree):
        residual = right_side - operate(solution)
        next_factor = 1.0 / (2.0 * sharpness - factor)
        update = next_factor * factor * update + 2.0 * next_factor / half_width * (
            scaled * residual
        )
        solution = solution + update
        factor = next_factor
    return solution


def merge_rims(extended, which_axis):
    length_here = extended.shape[which_axis]
    inner_part = lax.slice_in_dim(extended, 1, length_here - 1, axis=which_axis)
    below_rim = lax.slice_in_dim(extended, 0, 1, axis=which_axis)
    above_rim = lax.slice_in_dim(extended, length_here - 1, length_here, axis=which_axis)
    return (
        inner_part
        + pad_axis(below_rim, which_axis, 0, length_here - 3)
        + pad_axis(above_rim, which_axis, length_here - 3, 0)
    )


def merge_all(extended, axes_list):
    for which_axis in axes_list:
        extended = merge_rims(extended, which_axis)
    return extended


def faces_fine(stacked):
    extended = padded(stacked, (("gx", 3), ("gy", 2), ("gz", 1)), 1)
    return merge_all(extended, (1, 2, 3))


def coarse_sums(stacked):
    extended = padded(stacked, (("gx", 3), ("gy", 2), ("gz", 1)), 1)
    return merge_all(extended, (1, 2, 3))


def widened(stacked, sides, width):
    for axis, dim in sides:
        count = lax.axis_size(axis)
        length_here = stacked.shape[dim]
        head = lax.slice_in_dim(stacked, 0, width, axis=dim)
        tail = lax.slice_in_dim(stacked, length_here - width, length_here, axis=dim)
        below = lax.ppermute(tail, axis, [(i, (i + 1) % count) for i in range(count)])
        above = lax.ppermute(head, axis, [((i + 1) % count, i) for i in range(count)])
        stacked = jnp.concatenate(
            [
                lax.slice_in_dim(below, 0, width - 1, axis=dim),
                lax.slice_in_dim(below, width - 1, width, axis=dim)
                + lax.slice_in_dim(stacked, 0, 1, axis=dim),
                lax.slice_in_dim(stacked, 1, length_here - 1, axis=dim),
                lax.slice_in_dim(stacked, length_here - 1, length_here, axis=dim)
                + lax.slice_in_dim(above, 0, 1, axis=dim),
                lax.slice_in_dim(above, 1, width, axis=dim),
            ],
            axis=dim,
        )
    return stacked


def on_device(element_load, conductivity):
    load_full = pad_axis(element_load, 2, 0, 1)
    cond_nodes = jnp.zeros(load_full.shape, conductivity.dtype)
    cond_nodes = cond_nodes.at[:-1:2, :-1:2, :-1:2].set(conductivity)
    ring = 2
    wide = widened(
        jnp.stack([load_full, diag_local(conductivity, 1.0, reaction_rate), cond_nodes], 0),
        (("gx", 3), ("gy", 2), ("gz", 1)),
        ring + 1,
    )
    inner = wide[:, ring:-ring, ring:-ring, ring:-ring]
    right_side = inner[0]
    diagonal = inner[1]
    cells = conductivity.shape
    cond_wide = wide[2, : 2 * cells[0] + 3 : 2, : 2 * cells[1] + 3 : 2, : 2 * cells[2] + 3 : 2]

    def operate_fine(node_field):
        return faces_fine(apply_local(node_field, conductivity, 1.0, reaction_rate)[None])[0]

    centre = 0.5 * (upper_bound + lower_bound)
    half_width = 0.5 * (upper_bound - lower_bound)
    sharpness = centre / half_width
    factor = 1.0 / sharpness
    scaled = 1.0 / diagonal
    update = scaled * right_side * (1.0 / centre)
    smooth = update
    first_wide = 1.0 / wide[1] * wide[0] * (1.0 / centre)
    applied_first = apply_local(first_wide, cond_wide, 1.0, reaction_rate)[
        ring:-ring, ring:-ring, ring:-ring
    ]
    for k in range(1, DEG1):
        if k == 1:
            residual = right_side - applied_first
        else:
            residual = right_side - operate_fine(smooth)
        next_factor = 1.0 / (2.0 * sharpness - factor)
        update = next_factor * factor * update + 2.0 * next_factor / half_width * (
            scaled * residual
        )
        smooth = smooth + update
        factor = next_factor
    partial_value = load_full - apply_local(smooth, conductivity, 1.0, reaction_rate)
    coarse_load = restrict_all(partial_value)
    coarse_cond = coarse_conduct(conductivity)
    coarse_mass = 8.0 * reaction_rate
    coarse_diag = diag_local(coarse_cond, 2.0, coarse_mass)
    coarse_both = coarse_sums(jnp.stack([coarse_load, coarse_diag], 0))

    def operate_coarse(node_field):
        return coarse_sums(apply_local(node_field, coarse_cond, 2.0, coarse_mass)[None])[0]

    correction = chebyshev(coarse_both[0], coarse_both[1], operate_coarse, DEG2)
    corrected = smooth + prolong_all(correction)
    return corrected[:, :, : corrected.shape[2] - 1]


def solution(mesh):
    in_specs = (P("gz", "gy", "gx"), P("gz", "gy", "gx"))
    out_specs = P("gz", "gy", "gx")
    return jax.shard_map(
        on_device, mesh=mesh, in_specs=in_specs, out_specs=out_specs, check_vma=False
    )
```

```python
import jax
import jax.numpy as jnp
import numpy as np
from jax import lax
from jax.sharding import PartitionSpec as P

DEG1 = 3
DEG2 = 4


reaction_rate = 0.05
lower_bound = 0.25
upper_bound = 2.5
mass_table = [
    [4.0 / 30.0, 2.0 / 30.0, -1.0 / 30.0],
    [2.0 / 30.0, 16.0 / 30.0, 2.0 / 30.0],
    [-1.0 / 30.0, 2.0 / 30.0, 4.0 / 30.0],
]
stiff_table = [
    [7.0 / 3.0, -8.0 / 3.0, 1.0 / 3.0],
    [-8.0 / 3.0, 16.0 / 3.0, -8.0 / 3.0],
    [1.0 / 3.0, -8.0 / 3.0, 7.0 / 3.0],
]


def padded(cells, sides, width):
    for axis, dim in sides:
        count = lax.axis_size(axis)
        head = lax.slice_in_dim(cells, 0, width, axis=dim)
        tail = lax.slice_in_dim(cells, cells.shape[dim] - width, cells.shape[dim], axis=dim)
        cells = jnp.concatenate(
            [
                lax.ppermute(tail, axis, [(i, (i + 1) % count) for i in range(count)]),
                cells,
                lax.ppermute(head, axis, [((i + 1) % count, i) for i in range(count)]),
            ],
            axis=dim,
        )
    return cells


def pad_axis(values, which_axis, before, after):
    widths = [(0, 0)] * values.ndim
    widths[which_axis] = (before, after)
    return jnp.pad(values, widths)


def contract(values, matrix, which_axis):
    pieces = [lax.index_in_dim(values, a, which_axis, keepdims=False) for a in range(3)]
    results = [
        matrix[b][0] * pieces[0] + matrix[b][1] * pieces[1] + matrix[b][2] * pieces[2]
        for b in range(3)
    ]
    return jnp.stack(results, axis=which_axis)


def node_slices(node_field, which_axis):
    elements = (node_field.shape[which_axis] - 1) // 2
    return [
        lax.slice_in_dim(node_field, a, a + 2 * elements - 1, 2, axis=which_axis) for a in range(3)
    ]


def spread(node_field):
    length_x = node_field.shape[2]
    elements_x = (length_x - 1) // 2
    even_x = lax.slice_in_dim(node_field, 0, length_x, 2, axis=2)
    odd_x = lax.slice_in_dim(node_field, 1, length_x, 2, axis=2)
    along_x = jnp.stack(
        [
            lax.slice_in_dim(even_x, 0, elements_x, axis=2),
            odd_x,
            lax.slice_in_dim(even_x, 1, elements_x + 1, axis=2),
        ],
        0,
    )
    along_y = jnp.stack(node_slices(along_x, 2), 1)
    return jnp.stack(node_slices(along_y, 2), 2)


def fold_back(stacked, which_axis):
    lower_part = stacked[0]
    middle_part = stacked[1]
    upper_part = stacked[2]
    target = which_axis - 1
    elements = lower_part.shape[target]
    even_full = pad_axis(lower_part, target, 0, 1) + pad_axis(upper_part, target, 1, 0)
    even_nodes = lax.slice_in_dim(even_full, 0, elements, axis=target)
    tail_node = lax.slice_in_dim(even_full, elements, elements + 1, axis=target)
    woven_nodes = jnp.stack([even_nodes, middle_part], axis=target + 1)
    node_shape = list(even_nodes.shape)
    node_shape[target] = 2 * elements
    woven_nodes = woven_nodes.reshape(node_shape)
    return jnp.concatenate([woven_nodes, tail_node], axis=target)


def fold_local(stacked, local_dim, target):
    parts = [lax.index_in_dim(stacked, a, local_dim, keepdims=False) for a in range(3)]
    return fold_back(parts, target + 1)


def gather_elements(product):
    folded = fold_local(product, 2, 2)
    folded = fold_local(folded, 1, 2)
    return fold_local(folded, 0, 2)


def apply_local(node_field, conduct, stiff_scale, mass_scale):
    node_values = spread(node_field)
    mass_depth = contract(node_values, mass_table, 2)
    mass_plane = contract(mass_depth, mass_table, 1)
    stiffness = contract(mass_plane, stiff_table, 0)
    mass_width = contract(node_values, mass_table, 0)
    stiffness = stiffness + contract(contract(mass_width, stiff_table, 1), mass_table, 2)
    mass_face = contract(mass_width, mass_table, 1)
    stiffness = stiffness + contract(mass_face, stiff_table, 2)
    product = stiff_scale * conduct * stiffness + mass_scale * contract(mass_face, mass_table, 2)
    return gather_elements(product)


def diag_tables():
    stiff_line = np.array([stiff_table[a][a] for a in range(3)])
    mass_line = np.array([mass_table[a][a] for a in range(3)])
    stiff_part = (
        stiff_line[:, None, None] * mass_line[None, :, None] * mass_line[None, None, :]
        + mass_line[:, None, None] * stiff_line[None, :, None] * mass_line[None, None, :]
        + mass_line[:, None, None] * mass_line[None, :, None] * stiff_line[None, None, :]
    )
    mass_part = mass_line[:, None, None] * mass_line[None, :, None] * mass_line[None, None, :]
    return (stiff_part.reshape(3, 3, 3, 1, 1, 1), mass_part.reshape(3, 3, 3, 1, 1, 1))


def diag_local(conduct, stiff_scale, mass_scale):
    stiff_part, mass_part = diag_tables()
    product = stiff_scale * conduct * jnp.asarray(
        stiff_part, conduct.dtype
    ) + mass_scale * jnp.asarray(mass_part, conduct.dtype)
    return gather_elements(product)


def coarse_conduct(conduct):
    layers_z, rows_y, cols_x = conduct.shape
    shaped = conduct.reshape(layers_z // 2, 2, rows_y // 2, 2, cols_x // 2, 2)
    return jnp.sum(shaped, axis=(1, 3, 5)) * 0.125


def prolong_axis(coarse, which_axis):
    pieces = node_slices(coarse, which_axis)
    fine_parts = [
        pieces[0],
        0.375 * pieces[0] + 0.75 * pieces[1] - 0.125 * pieces[2],
        pieces[1],
        -0.125 * pieces[0] + 0.75 * pieces[1] + 0.375 * pieces[2],
    ]
    woven_nodes = jnp.stack(fine_parts, axis=which_axis + 1)
    node_shape = list(pieces[0].shape)
    node_shape[which_axis] = 4 * pieces[0].shape[which_axis]
    woven_nodes = woven_nodes.reshape(node_shape)
    length_here = coarse.shape[which_axis]
    tail_node = lax.slice_in_dim(coarse, length_here - 1, length_here, axis=which_axis)
    return jnp.concatenate([woven_nodes, tail_node], axis=which_axis)


def prolong_all(coarse):
    result = prolong_axis(coarse, 0)
    result = prolong_axis(result, 1)
    return prolong_axis(result, 2)


def restrict_axis(fine, which_axis):
    length_here = fine.shape[which_axis]
    elements = (length_here - 1) // 4
    quarters = [
        lax.slice_in_dim(fine, q, q + 4 * elements - 3, 4, axis=which_axis) for q in range(4)
    ]
    coarse_parts = [
        quarters[0] + 0.375 * quarters[1] - 0.125 * quarters[3],
        0.75 * quarters[1] + quarters[2] + 0.75 * quarters[3],
        -0.125 * quarters[1] + 0.375 * quarters[3],
    ]
    folded = fold_back(jnp.stack(coarse_parts, 0), which_axis + 1)
    tail_node = lax.slice_in_dim(fine, length_here - 1, length_here, axis=which_axis)
    return folded + pad_axis(tail_node, which_axis, 2 * elements, 0)


def restrict_all(fine):
    result = restrict_axis(fine, 0)
    result = restrict_axis(result, 1)
    return restrict_axis(result, 2)


def chebyshev(right_side, diagonal, operate, degree):
    centre = 0.5 * (upper_bound + lower_bound)
    half_width = 0.5 * (upper_bound - lower_bound)
    sharpness = centre / half_width
    factor = 1.0 / sharpness
    scaled = 1.0 / diagonal
    update = scaled * right_side * (1.0 / centre)
    solution = update
    for k in range(1, degree):
        residual = right_side - operate(solution)
        next_factor = 1.0 / (2.0 * sharpness - factor)
        update = next_factor * factor * update + 2.0 * next_factor / half_width * (
            scaled * residual
        )
        solution = solution + update
        factor = next_factor
    return solution


def merge_rims(extended, which_axis):
    length_here = extended.shape[which_axis]
    inner_part = lax.slice_in_dim(extended, 1, length_here - 1, axis=which_axis)
    below_rim = lax.slice_in_dim(extended, 0, 1, axis=which_axis)
    above_rim = lax.slice_in_dim(extended, length_here - 1, length_here, axis=which_axis)
    return (
        inner_part
        + pad_axis(below_rim, which_axis, 0, length_here - 3)
        + pad_axis(above_rim, which_axis, length_here - 3, 0)
    )


def merge_all(extended, axes_list):
    for which_axis in axes_list:
        extended = merge_rims(extended, which_axis)
    return extended


def faces_fine(stacked):
    extended = padded(stacked, (("gx", 3), ("gy", 2), ("gz", 1)), 1)
    return merge_all(extended, (1, 2, 3))


def coarse_sums(stacked):
    extended = padded(stacked, (("gx", 3), ("gy", 2), ("gz", 1)), 1)
    return merge_all(extended, (1, 2, 3))


def widened(stacked, sides, width):
    for axis, dim in sides:
        count = lax.axis_size(axis)
        length_here = stacked.shape[dim]
        head = lax.slice_in_dim(stacked, 0, width, axis=dim)
        tail = lax.slice_in_dim(stacked, length_here - width, length_here, axis=dim)
        below = lax.ppermute(tail, axis, [(i, (i + 1) % count) for i in range(count)])
        above = lax.ppermute(head, axis, [((i + 1) % count, i) for i in range(count)])
        stacked = jnp.concatenate(
            [
                lax.slice_in_dim(below, 0, width - 1, axis=dim),
                lax.slice_in_dim(below, width - 1, width, axis=dim)
                + lax.slice_in_dim(stacked, 0, 1, axis=dim),
                lax.slice_in_dim(stacked, 1, length_here - 1, axis=dim),
                lax.slice_in_dim(stacked, length_here - 1, length_here, axis=dim)
                + lax.slice_in_dim(above, 0, 1, axis=dim),
                lax.slice_in_dim(above, 1, width, axis=dim),
            ],
            axis=dim,
        )
    return stacked


def on_device(element_load, conductivity):
    load_full = pad_axis(element_load, 2, 0, 1)
    cond_nodes = jnp.zeros(load_full.shape, conductivity.dtype)
    cond_nodes = cond_nodes.at[:-1:2, :-1:2, :-1:2].set(conductivity)
    ring = 2
    wide = widened(
        jnp.stack([load_full, diag_local(conductivity, 1.0, reaction_rate), cond_nodes], 0),
        (("gx", 3), ("gy", 2), ("gz", 1)),
        ring + 1,
    )
    inner = wide[:, ring:-ring, ring:-ring, ring:-ring]
    right_side = inner[0]
    diagonal = inner[1]
    cells = conductivity.shape
    cond_wide = wide[2, : 2 * cells[0] + 3 : 2, : 2 * cells[1] + 3 : 2, : 2 * cells[2] + 3 : 2]

    def operate_fine(node_field):
        return faces_fine(apply_local(node_field, conductivity, 1.0, reaction_rate)[None])[0]

    centre = 0.5 * (upper_bound + lower_bound)
    half_width = 0.5 * (upper_bound - lower_bound)
    sharpness = centre / half_width
    factor = 1.0 / sharpness
    scaled = 1.0 / diagonal
    update = scaled * right_side * (1.0 / centre)
    smooth = update
    first_wide = 1.0 / wide[1] * wide[0] * (1.0 / centre)
    applied_first = apply_local(first_wide, cond_wide, 1.0, reaction_rate)[
        ring:-ring, ring:-ring, ring:-ring
    ]
    for k in range(1, DEG1):
        if k == 1:
            residual = right_side - applied_first
        else:
            residual = right_side - operate_fine(smooth)
        next_factor = 1.0 / (2.0 * sharpness - factor)
        update = next_factor * factor * update + 2.0 * next_factor / half_width * (
            scaled * residual
        )
        smooth = smooth + update
        factor = next_factor
    partial_value = load_full - apply_local(smooth, conductivity, 1.0, reaction_rate)
    coarse_load = restrict_all(partial_value)
    coarse_cond = coarse_conduct(conductivity)
    coarse_mass = 8.0 * reaction_rate
    coarse_diag = diag_local(coarse_cond, 2.0, coarse_mass)
    coarse_both = coarse_sums(jnp.stack([coarse_load, coarse_diag], 0))

    def operate_coarse(node_field):
        return coarse_sums(apply_local(node_field, coarse_cond, 2.0, coarse_mass)[None])[0]

    correction = chebyshev(coarse_both[0], coarse_both[1], operate_coarse, DEG2)
    corrected = smooth + prolong_all(correction)
    return corrected[:, :, : corrected.shape[2] - 1]


def solution(mesh):
    in_specs = (P("gz", "gy", "gx"), P("gz", "gy", "gx"))
    out_specs = P("gz", "gy", "gx")
    return jax.shard_map(
        on_device, mesh=mesh, in_specs=in_specs, out_specs=out_specs, check_vma=False
    )
```

```python
import jax
import jax.numpy as jnp
import numpy as np
from jax import lax
from jax.sharding import PartitionSpec as P

DEG1 = 3
DEG2 = 4


reaction_rate = 0.05
lower_bound = 0.25
upper_bound = 2.5
mass_table = [
    [4.0 / 30.0, 2.0 / 30.0, -1.0 / 30.0],
    [2.0 / 30.0, 16.0 / 30.0, 2.0 / 30.0],
    [-1.0 / 30.0, 2.0 / 30.0, 4.0 / 30.0],
]
stiff_table = [
    [7.0 / 3.0, -8.0 / 3.0, 1.0 / 3.0],
    [-8.0 / 3.0, 16.0 / 3.0, -8.0 / 3.0],
    [1.0 / 3.0, -8.0 / 3.0, 7.0 / 3.0],
]


def padded(cells, sides, width):
    for axis, dim in sides:
        count = lax.axis_size(axis)
        head = lax.slice_in_dim(cells, 0, width, axis=dim)
        tail = lax.slice_in_dim(cells, cells.shape[dim] - width, cells.shape[dim], axis=dim)
        cells = jnp.concatenate(
            [
                lax.ppermute(tail, axis, [(i, (i + 1) % count) for i in range(count)]),
                cells,
                lax.ppermute(head, axis, [((i + 1) % count, i) for i in range(count)]),
            ],
            axis=dim,
        )
    return cells


def pad_axis(values, which_axis, before, after):
    widths = [(0, 0)] * values.ndim
    widths[which_axis] = (before, after)
    return jnp.pad(values, widths)


def contract(values, matrix, which_axis):
    pieces = [lax.index_in_dim(values, a, which_axis, keepdims=False) for a in range(3)]
    results = [
        matrix[b][0] * pieces[0] + matrix[b][1] * pieces[1] + matrix[b][2] * pieces[2]
        for b in range(3)
    ]
    return jnp.stack(results, axis=which_axis)


def node_slices(node_field, which_axis):
    elements = (node_field.shape[which_axis] - 1) // 2
    return [
        lax.slice_in_dim(node_field, a, a + 2 * elements - 1, 2, axis=which_axis) for a in range(3)
    ]


def spread(node_field):
    length_x = node_field.shape[2]
    elements_x = (length_x - 1) // 2
    even_x = lax.slice_in_dim(node_field, 0, length_x, 2, axis=2)
    odd_x = lax.slice_in_dim(node_field, 1, length_x, 2, axis=2)
    along_x = jnp.stack(
        [
            lax.slice_in_dim(even_x, 0, elements_x, axis=2),
            odd_x,
            lax.slice_in_dim(even_x, 1, elements_x + 1, axis=2),
        ],
        0,
    )
    along_y = jnp.stack(node_slices(along_x, 2), 1)
    return jnp.stack(node_slices(along_y, 2), 2)


def fold_back(stacked, which_axis):
    lower_part = stacked[0]
    middle_part = stacked[1]
    upper_part = stacked[2]
    target = which_axis - 1
    elements = lower_part.shape[target]
    even_full = pad_axis(lower_part, target, 0, 1) + pad_axis(upper_part, target, 1, 0)
    even_nodes = lax.slice_in_dim(even_full, 0, elements, axis=target)
    tail_node = lax.slice_in_dim(even_full, elements, elements + 1, axis=target)
    woven_nodes = jnp.stack([even_nodes, middle_part], axis=target + 1)
    node_shape = list(even_nodes.shape)
    node_shape[target] = 2 * elements
    woven_nodes = woven_nodes.reshape(node_shape)
    return jnp.concatenate([woven_nodes, tail_node], axis=target)


def fold_local(stacked, local_dim, target):
    parts = [lax.index_in_dim(stacked, a, local_dim, keepdims=False) for a in range(3)]
    return fold_back(parts, target + 1)


def gather_elements(product):
    folded = fold_local(product, 2, 2)
    folded = fold_local(folded, 1, 2)
    return fold_local(folded, 0, 2)


def apply_local(node_field, conduct, stiff_scale, mass_scale):
    node_values = spread(node_field)
    mass_depth = contract(node_values, mass_table, 2)
    mass_plane = contract(mass_depth, mass_table, 1)
    stiffness = contract(mass_plane, stiff_table, 0)
    mass_width = contract(node_values, mass_table, 0)
    stiffness = stiffness + contract(contract(mass_width, stiff_table, 1), mass_table, 2)
    mass_face = contract(mass_width, mass_table, 1)
    stiffness = stiffness + contract(mass_face, stiff_table, 2)
    product = stiff_scale * conduct * stiffness + mass_scale * contract(mass_face, mass_table, 2)
    return gather_elements(product)


def diag_tables():
    stiff_line = np.array([stiff_table[a][a] for a in range(3)])
    mass_line = np.array([mass_table[a][a] for a in range(3)])
    stiff_part = (
        stiff_line[:, None, None] * mass_line[None, :, None] * mass_line[None, None, :]
        + mass_line[:, None, None] * stiff_line[None, :, None] * mass_line[None, None, :]
        + mass_line[:, None, None] * mass_line[None, :, None] * stiff_line[None, None, :]
    )
    mass_part = mass_line[:, None, None] * mass_line[None, :, None] * mass_line[None, None, :]
    return (stiff_part.reshape(3, 3, 3, 1, 1, 1), mass_part.reshape(3, 3, 3, 1, 1, 1))


def diag_local(conduct, stiff_scale, mass_scale):
    stiff_part, mass_part = diag_tables()
    product = stiff_scale * conduct * jnp.asarray(
        stiff_part, conduct.dtype
    ) + mass_scale * jnp.asarray(mass_part, conduct.dtype)
    return gather_elements(product)


def coarse_conduct(conduct):
    layers_z, rows_y, cols_x = conduct.shape
    shaped = conduct.reshape(layers_z // 2, 2, rows_y // 2, 2, cols_x // 2, 2)
    return jnp.sum(shaped, axis=(1, 3, 5)) * 0.125


def prolong_axis(coarse, which_axis):
    pieces = node_slices(coarse, which_axis)
    fine_parts = [
        pieces[0],
        0.375 * pieces[0] + 0.75 * pieces[1] - 0.125 * pieces[2],
        pieces[1],
        -0.125 * pieces[0] + 0.75 * pieces[1] + 0.375 * pieces[2],
    ]
    woven_nodes = jnp.stack(fine_parts, axis=which_axis + 1)
    node_shape = list(pieces[0].shape)
    node_shape[which_axis] = 4 * pieces[0].shape[which_axis]
    woven_nodes = woven_nodes.reshape(node_shape)
    length_here = coarse.shape[which_axis]
    tail_node = lax.slice_in_dim(coarse, length_here - 1, length_here, axis=which_axis)
    return jnp.concatenate([woven_nodes, tail_node], axis=which_axis)


def prolong_all(coarse):
    result = prolong_axis(coarse, 0)
    result = prolong_axis(result, 1)
    return prolong_axis(result, 2)


def restrict_axis(fine, which_axis):
    length_here = fine.shape[which_axis]
    elements = (length_here - 1) // 4
    quarters = [
        lax.slice_in_dim(fine, q, q + 4 * elements - 3, 4, axis=which_axis) for q in range(4)
    ]
    coarse_parts = [
        quarters[0] + 0.375 * quarters[1] - 0.125 * quarters[3],
        0.75 * quarters[1] + quarters[2] + 0.75 * quarters[3],
        -0.125 * quarters[1] + 0.375 * quarters[3],
    ]
    folded = fold_back(jnp.stack(coarse_parts, 0), which_axis + 1)
    tail_node = lax.slice_in_dim(fine, length_here - 1, length_here, axis=which_axis)
    return folded + pad_axis(tail_node, which_axis, 2 * elements, 0)


def restrict_all(fine):
    result = restrict_axis(fine, 0)
    result = restrict_axis(result, 1)
    return restrict_axis(result, 2)


def chebyshev(right_side, diagonal, operate, degree):
    centre = 0.5 * (upper_bound + lower_bound)
    half_width = 0.5 * (upper_bound - lower_bound)
    sharpness = centre / half_width
    factor = 1.0 / sharpness
    scaled = 1.0 / diagonal
    update = scaled * right_side * (1.0 / centre)
    solution = update
    for k in range(1, degree):
        residual = right_side - operate(solution)
        next_factor = 1.0 / (2.0 * sharpness - factor)
        update = next_factor * factor * update + 2.0 * next_factor / half_width * (
            scaled * residual
        )
        solution = solution + update
        factor = next_factor
    return solution


def merge_rims(extended, which_axis):
    length_here = extended.shape[which_axis]
    inner_part = lax.slice_in_dim(extended, 1, length_here - 1, axis=which_axis)
    below_rim = lax.slice_in_dim(extended, 0, 1, axis=which_axis)
    above_rim = lax.slice_in_dim(extended, length_here - 1, length_here, axis=which_axis)
    return (
        inner_part
        + pad_axis(below_rim, which_axis, 0, length_here - 3)
        + pad_axis(above_rim, which_axis, length_here - 3, 0)
    )


def merge_all(extended, axes_list):
    for which_axis in axes_list:
        extended = merge_rims(extended, which_axis)
    return extended


def faces_fine(stacked):
    extended = padded(stacked, (("gx", 3), ("gy", 2), ("gz", 1)), 1)
    return merge_all(extended, (1, 2, 3))


def coarse_sums(stacked):
    extended = padded(stacked, (("gx", 3), ("gy", 2), ("gz", 1)), 1)
    return merge_all(extended, (1, 2, 3))


def widened(stacked, sides, width):
    for axis, dim in sides:
        count = lax.axis_size(axis)
        length_here = stacked.shape[dim]
        head = lax.slice_in_dim(stacked, 0, width, axis=dim)
        tail = lax.slice_in_dim(stacked, length_here - width, length_here, axis=dim)
        below = lax.ppermute(tail, axis, [(i, (i + 1) % count) for i in range(count)])
        above = lax.ppermute(head, axis, [((i + 1) % count, i) for i in range(count)])
        stacked = jnp.concatenate(
            [
                lax.slice_in_dim(below, 0, width - 1, axis=dim),
                lax.slice_in_dim(below, width - 1, width, axis=dim)
                + lax.slice_in_dim(stacked, 0, 1, axis=dim),
                lax.slice_in_dim(stacked, 1, length_here - 1, axis=dim),
                lax.slice_in_dim(stacked, length_here - 1, length_here, axis=dim)
                + lax.slice_in_dim(above, 0, 1, axis=dim),
                lax.slice_in_dim(above, 1, width, axis=dim),
            ],
            axis=dim,
        )
    return stacked


def on_device(element_load, conductivity):
    load_full = pad_axis(element_load, 2, 0, 1)
    cond_nodes = lax.pad(
        conductivity, jnp.zeros((), conductivity.dtype), [(0, 2, 1), (0, 2, 1), (0, 2, 1)]
    )
    ring = 2
    wide = widened(
        jnp.stack([load_full, diag_local(conductivity, 1.0, reaction_rate), cond_nodes], 0),
        (("gx", 3), ("gy", 2), ("gz", 1)),
        ring + 1,
    )
    inner = wide[:, ring:-ring, ring:-ring, ring:-ring]
    right_side = inner[0]
    diagonal = inner[1]
    cells = conductivity.shape
    cond_wide = wide[2, : 2 * cells[0] + 3 : 2, : 2 * cells[1] + 3 : 2, : 2 * cells[2] + 3 : 2]

    def operate_fine(node_field):
        return faces_fine(apply_local(node_field, conductivity, 1.0, reaction_rate)[None])[0]

    centre = 0.5 * (upper_bound + lower_bound)
    half_width = 0.5 * (upper_bound - lower_bound)
    sharpness = centre / half_width
    factor = 1.0 / sharpness
    scaled = 1.0 / diagonal
    update = scaled * right_side * (1.0 / centre)
    smooth = update
    first_wide = 1.0 / wide[1] * wide[0] * (1.0 / centre)
    applied_first = apply_local(first_wide, cond_wide, 1.0, reaction_rate)[
        ring:-ring, ring:-ring, ring:-ring
    ]
    for k in range(1, DEG1):
        if k == 1:
            residual = right_side - applied_first
        else:
            residual = right_side - operate_fine(smooth)
        next_factor = 1.0 / (2.0 * sharpness - factor)
        update = next_factor * factor * update + 2.0 * next_factor / half_width * (
            scaled * residual
        )
        smooth = smooth + update
        factor = next_factor
    partial_value = load_full - apply_local(smooth, conductivity, 1.0, reaction_rate)
    coarse_load = restrict_all(partial_value)
    coarse_cond = coarse_conduct(conductivity)
    coarse_mass = 8.0 * reaction_rate
    coarse_diag = diag_local(coarse_cond, 2.0, coarse_mass)
    coarse_both = coarse_sums(jnp.stack([coarse_load, coarse_diag], 0))

    def operate_coarse(node_field):
        return coarse_sums(apply_local(node_field, coarse_cond, 2.0, coarse_mass)[None])[0]

    correction = chebyshev(coarse_both[0], coarse_both[1], operate_coarse, DEG2)
    corrected = smooth + prolong_all(correction)
    return corrected[:, :, : corrected.shape[2] - 1]


def solution(mesh):
    in_specs = (P("gz", "gy", "gx"), P("gz", "gy", "gx"))
    out_specs = P("gz", "gy", "gx")
    return jax.shard_map(
        on_device, mesh=mesh, in_specs=in_specs, out_specs=out_specs, check_vma=False
    )
```

```python
import jax
import jax.numpy as jnp
import numpy as np
from jax import lax
from jax.sharding import PartitionSpec as P

DEG1 = 3
DEG2 = 4


reaction_rate = 0.05
lower_bound = 0.25
upper_bound = 2.5
mass_table = [
    [4.0 / 30.0, 2.0 / 30.0, -1.0 / 30.0],
    [2.0 / 30.0, 16.0 / 30.0, 2.0 / 30.0],
    [-1.0 / 30.0, 2.0 / 30.0, 4.0 / 30.0],
]
stiff_table = [
    [7.0 / 3.0, -8.0 / 3.0, 1.0 / 3.0],
    [-8.0 / 3.0, 16.0 / 3.0, -8.0 / 3.0],
    [1.0 / 3.0, -8.0 / 3.0, 7.0 / 3.0],
]


def padded(cells, sides, width):
    for axis, dim in sides:
        count = lax.axis_size(axis)
        head = lax.slice_in_dim(cells, 0, width, axis=dim)
        tail = lax.slice_in_dim(cells, cells.shape[dim] - width, cells.shape[dim], axis=dim)
        cells = jnp.concatenate(
            [
                lax.ppermute(tail, axis, [(i, (i + 1) % count) for i in range(count)]),
                cells,
                lax.ppermute(head, axis, [((i + 1) % count, i) for i in range(count)]),
            ],
            axis=dim,
        )
    return cells


def pad_axis(values, which_axis, before, after):
    widths = [(0, 0)] * values.ndim
    widths[which_axis] = (before, after)
    return jnp.pad(values, widths)


def contract(values, matrix, which_axis):
    pieces = [lax.index_in_dim(values, a, which_axis, keepdims=False) for a in range(3)]
    results = [
        matrix[b][0] * pieces[0] + matrix[b][1] * pieces[1] + matrix[b][2] * pieces[2]
        for b in range(3)
    ]
    return jnp.stack(results, axis=which_axis)


def node_slices(node_field, which_axis):
    elements = (node_field.shape[which_axis] - 1) // 2
    return [
        lax.slice_in_dim(node_field, a, a + 2 * elements - 1, 2, axis=which_axis) for a in range(3)
    ]


def spread(node_field):
    length_x = node_field.shape[2]
    elements_x = (length_x - 1) // 2
    order = np.concatenate([np.arange(0, length_x, 2), np.arange(1, length_x, 2)])
    chooser = np.zeros((length_x, length_x), np.float32)
    chooser[order, np.arange(length_x)] = 1.0
    sorted_x = jnp.einsum(
        "zyx,xk->zyk", node_field, jnp.asarray(chooser), precision=lax.Precision.HIGHEST
    )
    even_x = lax.slice_in_dim(sorted_x, 0, elements_x + 1, axis=2)
    odd_x = lax.slice_in_dim(sorted_x, elements_x + 1, length_x, axis=2)
    along_x = jnp.stack(
        [
            lax.slice_in_dim(even_x, 0, elements_x, axis=2),
            odd_x,
            lax.slice_in_dim(even_x, 1, elements_x + 1, axis=2),
        ],
        0,
    )
    along_y = jnp.stack(node_slices(along_x, 2), 1)
    return jnp.stack(node_slices(along_y, 2), 2)


def fold_back(stacked, which_axis):
    lower_part = stacked[0]
    middle_part = stacked[1]
    upper_part = stacked[2]
    target = which_axis - 1
    elements = lower_part.shape[target]
    even_full = pad_axis(lower_part, target, 0, 1) + pad_axis(upper_part, target, 1, 0)
    even_nodes = lax.slice_in_dim(even_full, 0, elements, axis=target)
    tail_node = lax.slice_in_dim(even_full, elements, elements + 1, axis=target)
    woven_nodes = jnp.stack([even_nodes, middle_part], axis=target + 1)
    node_shape = list(even_nodes.shape)
    node_shape[target] = 2 * elements
    woven_nodes = woven_nodes.reshape(node_shape)
    return jnp.concatenate([woven_nodes, tail_node], axis=target)


def fold_local(stacked, local_dim, target):
    parts = [lax.index_in_dim(stacked, a, local_dim, keepdims=False) for a in range(3)]
    return fold_back(parts, target + 1)


def gather_elements(product):
    folded = fold_local(product, 2, 2)
    folded = fold_local(folded, 1, 2)
    return fold_local(folded, 0, 2)


def apply_local(node_field, conduct, stiff_scale, mass_scale):
    node_values = spread(node_field)
    mass_depth = contract(node_values, mass_table, 2)
    mass_plane = contract(mass_depth, mass_table, 1)
    stiffness = contract(mass_plane, stiff_table, 0)
    mass_width = contract(node_values, mass_table, 0)
    stiffness = stiffness + contract(contract(mass_width, stiff_table, 1), mass_table, 2)
    mass_face = contract(mass_width, mass_table, 1)
    stiffness = stiffness + contract(mass_face, stiff_table, 2)
    product = stiff_scale * conduct * stiffness + mass_scale * contract(mass_face, mass_table, 2)
    return gather_elements(product)


def diag_tables():
    stiff_line = np.array([stiff_table[a][a] for a in range(3)])
    mass_line = np.array([mass_table[a][a] for a in range(3)])
    stiff_part = (
        stiff_line[:, None, None] * mass_line[None, :, None] * mass_line[None, None, :]
        + mass_line[:, None, None] * stiff_line[None, :, None] * mass_line[None, None, :]
        + mass_line[:, None, None] * mass_line[None, :, None] * stiff_line[None, None, :]
    )
    mass_part = mass_line[:, None, None] * mass_line[None, :, None] * mass_line[None, None, :]
    return (stiff_part.reshape(3, 3, 3, 1, 1, 1), mass_part.reshape(3, 3, 3, 1, 1, 1))


def diag_local(conduct, stiff_scale, mass_scale):
    stiff_part, mass_part = diag_tables()
    product = stiff_scale * conduct * jnp.asarray(
        stiff_part, conduct.dtype
    ) + mass_scale * jnp.asarray(mass_part, conduct.dtype)
    return gather_elements(product)


def coarse_conduct(conduct):
    layers_z, rows_y, cols_x = conduct.shape
    shaped = conduct.reshape(layers_z // 2, 2, rows_y // 2, 2, cols_x // 2, 2)
    return jnp.sum(shaped, axis=(1, 3, 5)) * 0.125


def prolong_axis(coarse, which_axis):
    pieces = node_slices(coarse, which_axis)
    fine_parts = [
        pieces[0],
        0.375 * pieces[0] + 0.75 * pieces[1] - 0.125 * pieces[2],
        pieces[1],
        -0.125 * pieces[0] + 0.75 * pieces[1] + 0.375 * pieces[2],
    ]
    woven_nodes = jnp.stack(fine_parts, axis=which_axis + 1)
    node_shape = list(pieces[0].shape)
    node_shape[which_axis] = 4 * pieces[0].shape[which_axis]
    woven_nodes = woven_nodes.reshape(node_shape)
    length_here = coarse.shape[which_axis]
    tail_node = lax.slice_in_dim(coarse, length_here - 1, length_here, axis=which_axis)
    return jnp.concatenate([woven_nodes, tail_node], axis=which_axis)


def prolong_all(coarse):
    result = prolong_axis(coarse, 0)
    result = prolong_axis(result, 1)
    return prolong_axis(result, 2)


def restrict_axis(fine, which_axis):
    length_here = fine.shape[which_axis]
    elements = (length_here - 1) // 4
    quarters = [
        lax.slice_in_dim(fine, q, q + 4 * elements - 3, 4, axis=which_axis) for q in range(4)
    ]
    coarse_parts = [
        quarters[0] + 0.375 * quarters[1] - 0.125 * quarters[3],
        0.75 * quarters[1] + quarters[2] + 0.75 * quarters[3],
        -0.125 * quarters[1] + 0.375 * quarters[3],
    ]
    folded = fold_back(jnp.stack(coarse_parts, 0), which_axis + 1)
    tail_node = lax.slice_in_dim(fine, length_here - 1, length_here, axis=which_axis)
    return folded + pad_axis(tail_node, which_axis, 2 * elements, 0)


def restrict_all(fine):
    result = restrict_axis(fine, 0)
    result = restrict_axis(result, 1)
    return restrict_axis(result, 2)


def chebyshev(right_side, diagonal, operate, degree):
    centre = 0.5 * (upper_bound + lower_bound)
    half_width = 0.5 * (upper_bound - lower_bound)
    sharpness = centre / half_width
    factor = 1.0 / sharpness
    scaled = 1.0 / diagonal
    update = scaled * right_side * (1.0 / centre)
    solution = update
    for k in range(1, degree):
        residual = right_side - operate(solution)
        next_factor = 1.0 / (2.0 * sharpness - factor)
        update = next_factor * factor * update + 2.0 * next_factor / half_width * (
            scaled * residual
        )
        solution = solution + update
        factor = next_factor
    return solution


def merge_rims(extended, which_axis):
    length_here = extended.shape[which_axis]
    inner_part = lax.slice_in_dim(extended, 1, length_here - 1, axis=which_axis)
    below_rim = lax.slice_in_dim(extended, 0, 1, axis=which_axis)
    above_rim = lax.slice_in_dim(extended, length_here - 1, length_here, axis=which_axis)
    return (
        inner_part
        + pad_axis(below_rim, which_axis, 0, length_here - 3)
        + pad_axis(above_rim, which_axis, length_here - 3, 0)
    )


def merge_all(extended, axes_list):
    for which_axis in axes_list:
        extended = merge_rims(extended, which_axis)
    return extended


def faces_fine(stacked):
    extended = padded(stacked, (("gx", 3), ("gy", 2), ("gz", 1)), 1)
    return merge_all(extended, (1, 2, 3))


def coarse_sums(stacked):
    extended = padded(stacked, (("gx", 3), ("gy", 2), ("gz", 1)), 1)
    return merge_all(extended, (1, 2, 3))


def widened(stacked, sides, width):
    for axis, dim in sides:
        count = lax.axis_size(axis)
        length_here = stacked.shape[dim]
        head = lax.slice_in_dim(stacked, 0, width, axis=dim)
        tail = lax.slice_in_dim(stacked, length_here - width, length_here, axis=dim)
        below = lax.ppermute(tail, axis, [(i, (i + 1) % count) for i in range(count)])
        above = lax.ppermute(head, axis, [((i + 1) % count, i) for i in range(count)])
        stacked = jnp.concatenate(
            [
                lax.slice_in_dim(below, 0, width - 1, axis=dim),
                lax.slice_in_dim(below, width - 1, width, axis=dim)
                + lax.slice_in_dim(stacked, 0, 1, axis=dim),
                lax.slice_in_dim(stacked, 1, length_here - 1, axis=dim),
                lax.slice_in_dim(stacked, length_here - 1, length_here, axis=dim)
                + lax.slice_in_dim(above, 0, 1, axis=dim),
                lax.slice_in_dim(above, 1, width, axis=dim),
            ],
            axis=dim,
        )
    return stacked


def on_device(element_load, conductivity):
    load_full = pad_axis(element_load, 2, 0, 1)
    cond_nodes = lax.pad(
        conductivity, jnp.zeros((), conductivity.dtype), [(0, 2, 1), (0, 2, 1), (0, 2, 1)]
    )
    ring = 2
    wide = widened(
        jnp.stack([load_full, diag_local(conductivity, 1.0, reaction_rate), cond_nodes], 0),
        (("gx", 3), ("gy", 2), ("gz", 1)),
        ring + 1,
    )
    inner = wide[:, ring:-ring, ring:-ring, ring:-ring]
    right_side = inner[0]
    diagonal = inner[1]
    cells = conductivity.shape
    cond_wide = wide[2, : 2 * cells[0] + 3 : 2, : 2 * cells[1] + 3 : 2, : 2 * cells[2] + 3 : 2]

    def operate_fine(node_field):
        return faces_fine(apply_local(node_field, conductivity, 1.0, reaction_rate)[None])[0]

    centre = 0.5 * (upper_bound + lower_bound)
    half_width = 0.5 * (upper_bound - lower_bound)
    sharpness = centre / half_width
    factor = 1.0 / sharpness
    scaled = 1.0 / diagonal
    update = scaled * right_side * (1.0 / centre)
    smooth = update
    first_wide = 1.0 / wide[1] * wide[0] * (1.0 / centre)
    applied_first = apply_local(first_wide, cond_wide, 1.0, reaction_rate)[
        ring:-ring, ring:-ring, ring:-ring
    ]
    for k in range(1, DEG1):
        if k == 1:
            residual = right_side - applied_first
        else:
            residual = right_side - operate_fine(smooth)
        next_factor = 1.0 / (2.0 * sharpness - factor)
        update = next_factor * factor * update + 2.0 * next_factor / half_width * (
            scaled * residual
        )
        smooth = smooth + update
        factor = next_factor
    partial_value = load_full - apply_local(smooth, conductivity, 1.0, reaction_rate)
    coarse_load = restrict_all(partial_value)
    coarse_cond = coarse_conduct(conductivity)
    coarse_mass = 8.0 * reaction_rate
    coarse_diag = diag_local(coarse_cond, 2.0, coarse_mass)
    coarse_both = coarse_sums(jnp.stack([coarse_load, coarse_diag], 0))

    def operate_coarse(node_field):
        return coarse_sums(apply_local(node_field, coarse_cond, 2.0, coarse_mass)[None])[0]

    correction = chebyshev(coarse_both[0], coarse_both[1], operate_coarse, DEG2)
    corrected = smooth + prolong_all(correction)
    return corrected[:, :, : corrected.shape[2] - 1]


def solution(mesh):
    in_specs = (P("gz", "gy", "gx"), P("gz", "gy", "gx"))
    out_specs = P("gz", "gy", "gx")
    return jax.shard_map(
        on_device, mesh=mesh, in_specs=in_specs, out_specs=out_specs, check_vma=False
    )
```

```python
import jax
import jax.numpy as jnp
import numpy as np
from jax import lax
from jax.sharding import PartitionSpec as P

DEG1 = 3
DEG2 = 4


reaction_rate = 0.05
lower_bound = 0.25
upper_bound = 2.5
mass_table = [
    [4.0 / 30.0, 2.0 / 30.0, -1.0 / 30.0],
    [2.0 / 30.0, 16.0 / 30.0, 2.0 / 30.0],
    [-1.0 / 30.0, 2.0 / 30.0, 4.0 / 30.0],
]
stiff_table = [
    [7.0 / 3.0, -8.0 / 3.0, 1.0 / 3.0],
    [-8.0 / 3.0, 16.0 / 3.0, -8.0 / 3.0],
    [1.0 / 3.0, -8.0 / 3.0, 7.0 / 3.0],
]


def padded(cells, sides, width):
    for axis, dim in sides:
        count = lax.axis_size(axis)
        head = lax.slice_in_dim(cells, 0, width, axis=dim)
        tail = lax.slice_in_dim(cells, cells.shape[dim] - width, cells.shape[dim], axis=dim)
        cells = jnp.concatenate(
            [
                lax.ppermute(tail, axis, [(i, (i + 1) % count) for i in range(count)]),
                cells,
                lax.ppermute(head, axis, [((i + 1) % count, i) for i in range(count)]),
            ],
            axis=dim,
        )
    return cells


def pad_axis(values, which_axis, before, after):
    widths = [(0, 0)] * values.ndim
    widths[which_axis] = (before, after)
    return jnp.pad(values, widths)


def contract(values, matrix, which_axis):
    pieces = [lax.index_in_dim(values, a, which_axis, keepdims=False) for a in range(3)]
    results = [
        matrix[b][0] * pieces[0] + matrix[b][1] * pieces[1] + matrix[b][2] * pieces[2]
        for b in range(3)
    ]
    return jnp.stack(results, axis=which_axis)


def node_slices(node_field, which_axis):
    elements = (node_field.shape[which_axis] - 1) // 2
    return [
        lax.slice_in_dim(node_field, a, a + 2 * elements - 1, 2, axis=which_axis) for a in range(3)
    ]


def spread(node_field):
    length_x = node_field.shape[2]
    elements_x = (length_x - 1) // 2
    if node_field.shape[0] * node_field.shape[1] > 128:
        order = np.concatenate([np.arange(0, length_x, 2), np.arange(1, length_x, 2)])
        chooser = np.zeros((length_x, length_x), np.float32)
        chooser[order, np.arange(length_x)] = 1.0
        sorted_x = jnp.einsum(
            "zyx,xk->zyk", node_field, jnp.asarray(chooser), precision=lax.Precision.HIGHEST
        )
        even_x = lax.slice_in_dim(sorted_x, 0, elements_x + 1, axis=2)
        odd_x = lax.slice_in_dim(sorted_x, elements_x + 1, length_x, axis=2)
    else:
        even_x = lax.slice_in_dim(node_field, 0, length_x, 2, axis=2)
        odd_x = lax.slice_in_dim(node_field, 1, length_x, 2, axis=2)
    along_x = jnp.stack(
        [
            lax.slice_in_dim(even_x, 0, elements_x, axis=2),
            odd_x,
            lax.slice_in_dim(even_x, 1, elements_x + 1, axis=2),
        ],
        0,
    )
    along_y = jnp.stack(node_slices(along_x, 2), 1)
    return jnp.stack(node_slices(along_y, 2), 2)


def fold_back(stacked, which_axis):
    lower_part = stacked[0]
    middle_part = stacked[1]
    upper_part = stacked[2]
    target = which_axis - 1
    elements = lower_part.shape[target]
    even_full = pad_axis(lower_part, target, 0, 1) + pad_axis(upper_part, target, 1, 0)
    even_nodes = lax.slice_in_dim(even_full, 0, elements, axis=target)
    tail_node = lax.slice_in_dim(even_full, elements, elements + 1, axis=target)
    woven_nodes = jnp.stack([even_nodes, middle_part], axis=target + 1)
    node_shape = list(even_nodes.shape)
    node_shape[target] = 2 * elements
    woven_nodes = woven_nodes.reshape(node_shape)
    return jnp.concatenate([woven_nodes, tail_node], axis=target)


def fold_local(stacked, local_dim, target):
    parts = [lax.index_in_dim(stacked, a, local_dim, keepdims=False) for a in range(3)]
    return fold_back(parts, target + 1)


def gather_elements(product):
    folded = fold_local(product, 2, 2)
    folded = fold_local(folded, 1, 2)
    return fold_local(folded, 0, 2)


def apply_local(node_field, conduct, stiff_scale, mass_scale):
    node_values = spread(node_field)
    mass_depth = contract(node_values, mass_table, 2)
    mass_plane = contract(mass_depth, mass_table, 1)
    stiffness = contract(mass_plane, stiff_table, 0)
    mass_width = contract(node_values, mass_table, 0)
    stiffness = stiffness + contract(contract(mass_width, stiff_table, 1), mass_table, 2)
    mass_face = contract(mass_width, mass_table, 1)
    stiffness = stiffness + contract(mass_face, stiff_table, 2)
    product = stiff_scale * conduct * stiffness + mass_scale * contract(mass_face, mass_table, 2)
    return gather_elements(product)


def diag_tables():
    stiff_line = np.array([stiff_table[a][a] for a in range(3)])
    mass_line = np.array([mass_table[a][a] for a in range(3)])
    stiff_part = (
        stiff_line[:, None, None] * mass_line[None, :, None] * mass_line[None, None, :]
        + mass_line[:, None, None] * stiff_line[None, :, None] * mass_line[None, None, :]
        + mass_line[:, None, None] * mass_line[None, :, None] * stiff_line[None, None, :]
    )
    mass_part = mass_line[:, None, None] * mass_line[None, :, None] * mass_line[None, None, :]
    return (stiff_part.reshape(3, 3, 3, 1, 1, 1), mass_part.reshape(3, 3, 3, 1, 1, 1))


def diag_local(conduct, stiff_scale, mass_scale):
    stiff_part, mass_part = diag_tables()
    product = stiff_scale * conduct * jnp.asarray(
        stiff_part, conduct.dtype
    ) + mass_scale * jnp.asarray(mass_part, conduct.dtype)
    return gather_elements(product)


def coarse_conduct(conduct):
    layers_z, rows_y, cols_x = conduct.shape
    shaped = conduct.reshape(layers_z // 2, 2, rows_y // 2, 2, cols_x // 2, 2)
    return jnp.sum(shaped, axis=(1, 3, 5)) * 0.125


def prolong_axis(coarse, which_axis):
    pieces = node_slices(coarse, which_axis)
    fine_parts = [
        pieces[0],
        0.375 * pieces[0] + 0.75 * pieces[1] - 0.125 * pieces[2],
        pieces[1],
        -0.125 * pieces[0] + 0.75 * pieces[1] + 0.375 * pieces[2],
    ]
    woven_nodes = jnp.stack(fine_parts, axis=which_axis + 1)
    node_shape = list(pieces[0].shape)
    node_shape[which_axis] = 4 * pieces[0].shape[which_axis]
    woven_nodes = woven_nodes.reshape(node_shape)
    length_here = coarse.shape[which_axis]
    tail_node = lax.slice_in_dim(coarse, length_here - 1, length_here, axis=which_axis)
    return jnp.concatenate([woven_nodes, tail_node], axis=which_axis)


def prolong_all(coarse):
    result = prolong_axis(coarse, 0)
    result = prolong_axis(result, 1)
    return prolong_axis(result, 2)


def restrict_axis(fine, which_axis):
    length_here = fine.shape[which_axis]
    elements = (length_here - 1) // 4
    quarters = [
        lax.slice_in_dim(fine, q, q + 4 * elements - 3, 4, axis=which_axis) for q in range(4)
    ]
    coarse_parts = [
        quarters[0] + 0.375 * quarters[1] - 0.125 * quarters[3],
        0.75 * quarters[1] + quarters[2] + 0.75 * quarters[3],
        -0.125 * quarters[1] + 0.375 * quarters[3],
    ]
    folded = fold_back(jnp.stack(coarse_parts, 0), which_axis + 1)
    tail_node = lax.slice_in_dim(fine, length_here - 1, length_here, axis=which_axis)
    return folded + pad_axis(tail_node, which_axis, 2 * elements, 0)


def restrict_all(fine):
    result = restrict_axis(fine, 0)
    result = restrict_axis(result, 1)
    return restrict_axis(result, 2)


def chebyshev(right_side, diagonal, operate, degree):
    centre = 0.5 * (upper_bound + lower_bound)
    half_width = 0.5 * (upper_bound - lower_bound)
    sharpness = centre / half_width
    factor = 1.0 / sharpness
    scaled = 1.0 / diagonal
    update = scaled * right_side * (1.0 / centre)
    solution = update
    for k in range(1, degree):
        residual = right_side - operate(solution)
        next_factor = 1.0 / (2.0 * sharpness - factor)
        update = next_factor * factor * update + 2.0 * next_factor / half_width * (
            scaled * residual
        )
        solution = solution + update
        factor = next_factor
    return solution


def merge_rims(extended, which_axis):
    length_here = extended.shape[which_axis]
    inner_part = lax.slice_in_dim(extended, 1, length_here - 1, axis=which_axis)
    below_rim = lax.slice_in_dim(extended, 0, 1, axis=which_axis)
    above_rim = lax.slice_in_dim(extended, length_here - 1, length_here, axis=which_axis)
    return (
        inner_part
        + pad_axis(below_rim, which_axis, 0, length_here - 3)
        + pad_axis(above_rim, which_axis, length_here - 3, 0)
    )


def merge_all(extended, axes_list):
    for which_axis in axes_list:
        extended = merge_rims(extended, which_axis)
    return extended


def faces_fine(stacked):
    extended = padded(stacked, (("gx", 3), ("gy", 2), ("gz", 1)), 1)
    return merge_all(extended, (1, 2, 3))


def coarse_sums(stacked):
    extended = padded(stacked, (("gx", 3), ("gy", 2), ("gz", 1)), 1)
    return merge_all(extended, (1, 2, 3))


def widened(stacked, sides, width):
    for axis, dim in sides:
        count = lax.axis_size(axis)
        length_here = stacked.shape[dim]
        head = lax.slice_in_dim(stacked, 0, width, axis=dim)
        tail = lax.slice_in_dim(stacked, length_here - width, length_here, axis=dim)
        below = lax.ppermute(tail, axis, [(i, (i + 1) % count) for i in range(count)])
        above = lax.ppermute(head, axis, [((i + 1) % count, i) for i in range(count)])
        stacked = jnp.concatenate(
            [
                lax.slice_in_dim(below, 0, width - 1, axis=dim),
                lax.slice_in_dim(below, width - 1, width, axis=dim)
                + lax.slice_in_dim(stacked, 0, 1, axis=dim),
                lax.slice_in_dim(stacked, 1, length_here - 1, axis=dim),
                lax.slice_in_dim(stacked, length_here - 1, length_here, axis=dim)
                + lax.slice_in_dim(above, 0, 1, axis=dim),
                lax.slice_in_dim(above, 1, width, axis=dim),
            ],
            axis=dim,
        )
    return stacked


def on_device(element_load, conductivity):
    load_full = pad_axis(element_load, 2, 0, 1)
    cond_nodes = lax.pad(
        conductivity, jnp.zeros((), conductivity.dtype), [(0, 2, 1), (0, 2, 1), (0, 2, 1)]
    )
    ring = 2
    wide = widened(
        jnp.stack([load_full, diag_local(conductivity, 1.0, reaction_rate), cond_nodes], 0),
        (("gx", 3), ("gy", 2), ("gz", 1)),
        ring + 1,
    )
    inner = wide[:, ring:-ring, ring:-ring, ring:-ring]
    right_side = inner[0]
    diagonal = inner[1]
    cells = conductivity.shape
    cond_wide = wide[2, : 2 * cells[0] + 3 : 2, : 2 * cells[1] + 3 : 2, : 2 * cells[2] + 3 : 2]

    def operate_fine(node_field):
        return faces_fine(apply_local(node_field, conductivity, 1.0, reaction_rate)[None])[0]

    centre = 0.5 * (upper_bound + lower_bound)
    half_width = 0.5 * (upper_bound - lower_bound)
    sharpness = centre / half_width
    factor = 1.0 / sharpness
    scaled = 1.0 / diagonal
    update = scaled * right_side * (1.0 / centre)
    smooth = update
    first_wide = 1.0 / wide[1] * wide[0] * (1.0 / centre)
    applied_first = apply_local(first_wide, cond_wide, 1.0, reaction_rate)[
        ring:-ring, ring:-ring, ring:-ring
    ]
    for k in range(1, DEG1):
        if k == 1:
            residual = right_side - applied_first
        else:
            residual = right_side - operate_fine(smooth)
        next_factor = 1.0 / (2.0 * sharpness - factor)
        update = next_factor * factor * update + 2.0 * next_factor / half_width * (
            scaled * residual
        )
        smooth = smooth + update
        factor = next_factor
    partial_value = load_full - apply_local(smooth, conductivity, 1.0, reaction_rate)
    coarse_load = restrict_all(partial_value)
    coarse_cond = coarse_conduct(conductivity)
    coarse_mass = 8.0 * reaction_rate
    coarse_diag = diag_local(coarse_cond, 2.0, coarse_mass)
    coarse_both = coarse_sums(jnp.stack([coarse_load, coarse_diag], 0))

    def operate_coarse(node_field):
        return coarse_sums(apply_local(node_field, coarse_cond, 2.0, coarse_mass)[None])[0]

    correction = chebyshev(coarse_both[0], coarse_both[1], operate_coarse, DEG2)
    corrected = smooth + prolong_all(correction)
    return corrected[:, :, : corrected.shape[2] - 1]


def solution(mesh):
    in_specs = (P("gz", "gy", "gx"), P("gz", "gy", "gx"))
    out_specs = P("gz", "gy", "gx")
    return jax.shard_map(
        on_device, mesh=mesh, in_specs=in_specs, out_specs=out_specs, check_vma=False
    )
```

```python
import jax
import jax.numpy as jnp
import numpy as np
from jax import lax
from jax.sharding import PartitionSpec as P

DEG1 = 3
DEG2 = 4


reaction_rate = 0.05
lower_bound = 0.25
upper_bound = 2.5
mass_table = [
    [4.0 / 30.0, 2.0 / 30.0, -1.0 / 30.0],
    [2.0 / 30.0, 16.0 / 30.0, 2.0 / 30.0],
    [-1.0 / 30.0, 2.0 / 30.0, 4.0 / 30.0],
]
stiff_table = [
    [7.0 / 3.0, -8.0 / 3.0, 1.0 / 3.0],
    [-8.0 / 3.0, 16.0 / 3.0, -8.0 / 3.0],
    [1.0 / 3.0, -8.0 / 3.0, 7.0 / 3.0],
]


def padded(cells, sides, width):
    for axis, dim in sides:
        count = lax.axis_size(axis)
        head = lax.slice_in_dim(cells, 0, width, axis=dim)
        tail = lax.slice_in_dim(cells, cells.shape[dim] - width, cells.shape[dim], axis=dim)
        cells = jnp.concatenate(
            [
                lax.ppermute(tail, axis, [(i, (i + 1) % count) for i in range(count)]),
                cells,
                lax.ppermute(head, axis, [((i + 1) % count, i) for i in range(count)]),
            ],
            axis=dim,
        )
    return cells


def pad_axis(values, which_axis, before, after):
    widths = [(0, 0)] * values.ndim
    widths[which_axis] = (before, after)
    return jnp.pad(values, widths)


def contract(values, matrix, which_axis):
    pieces = [lax.index_in_dim(values, a, which_axis, keepdims=False) for a in range(3)]
    results = [
        matrix[b][0] * pieces[0] + matrix[b][1] * pieces[1] + matrix[b][2] * pieces[2]
        for b in range(3)
    ]
    return jnp.stack(results, axis=which_axis)


def node_slices(node_field, which_axis):
    elements = (node_field.shape[which_axis] - 1) // 2
    return [
        lax.slice_in_dim(node_field, a, a + 2 * elements - 1, 2, axis=which_axis) for a in range(3)
    ]


def spread(node_field):
    length_x = node_field.shape[2]
    elements_x = (length_x - 1) // 2
    if node_field.shape[0] * node_field.shape[1] > 128:
        order = np.concatenate([np.arange(0, length_x, 2), np.arange(1, length_x, 2)])
        chooser = np.zeros((length_x, length_x), np.float32)
        chooser[order, np.arange(length_x)] = 1.0
        sorted_x = jnp.einsum(
            "zyx,xk->zyk", node_field, jnp.asarray(chooser), precision=lax.Precision.HIGHEST
        )
        even_x = lax.slice_in_dim(sorted_x, 0, elements_x + 1, axis=2)
        odd_x = lax.slice_in_dim(sorted_x, elements_x + 1, length_x, axis=2)
    else:
        even_x = lax.slice_in_dim(node_field, 0, length_x, 2, axis=2)
        odd_x = lax.slice_in_dim(node_field, 1, length_x, 2, axis=2)
    along_x = jnp.stack(
        [
            lax.slice_in_dim(even_x, 0, elements_x, axis=2),
            odd_x,
            lax.slice_in_dim(even_x, 1, elements_x + 1, axis=2),
        ],
        0,
    )
    along_y = jnp.stack(node_slices(along_x, 2), 1)
    return jnp.stack(node_slices(along_y, 2), 2)


def fold_back(stacked, which_axis):
    lower_part = stacked[0]
    middle_part = stacked[1]
    upper_part = stacked[2]
    target = which_axis - 1
    elements = lower_part.shape[target]
    even_full = pad_axis(lower_part, target, 0, 1) + pad_axis(upper_part, target, 1, 0)
    even_nodes = lax.slice_in_dim(even_full, 0, elements, axis=target)
    tail_node = lax.slice_in_dim(even_full, elements, elements + 1, axis=target)
    woven_nodes = jnp.stack([even_nodes, middle_part], axis=target + 1)
    node_shape = list(even_nodes.shape)
    node_shape[target] = 2 * elements
    woven_nodes = woven_nodes.reshape(node_shape)
    return jnp.concatenate([woven_nodes, tail_node], axis=target)


def fold_local(stacked, local_dim, target):
    parts = [lax.index_in_dim(stacked, a, local_dim, keepdims=False) for a in range(3)]
    return fold_back(parts, target + 1)


def gather_elements(product):
    folded = fold_local(product, 2, 2)
    folded = fold_local(folded, 1, 2)
    return fold_local(folded, 0, 2)


def apply_local(node_field, conduct, stiff_scale, mass_scale):
    node_values = spread(node_field)
    mass_depth = contract(node_values, mass_table, 2)
    mass_plane = contract(mass_depth, mass_table, 1)
    stiffness = contract(mass_plane, stiff_table, 0)
    mass_width = contract(node_values, mass_table, 0)
    stiffness = stiffness + contract(contract(mass_width, stiff_table, 1), mass_table, 2)
    mass_face = contract(mass_width, mass_table, 1)
    stiffness = stiffness + contract(mass_face, stiff_table, 2)
    product = stiff_scale * conduct * stiffness + mass_scale * contract(mass_face, mass_table, 2)
    return gather_elements(product)


def diag_tables():
    stiff_line = np.array([stiff_table[a][a] for a in range(3)])
    mass_line = np.array([mass_table[a][a] for a in range(3)])
    stiff_part = (
        stiff_line[:, None, None] * mass_line[None, :, None] * mass_line[None, None, :]
        + mass_line[:, None, None] * stiff_line[None, :, None] * mass_line[None, None, :]
        + mass_line[:, None, None] * mass_line[None, :, None] * stiff_line[None, None, :]
    )
    mass_part = mass_line[:, None, None] * mass_line[None, :, None] * mass_line[None, None, :]
    return (stiff_part.reshape(3, 3, 3, 1, 1, 1), mass_part.reshape(3, 3, 3, 1, 1, 1))


def diag_local(conduct, stiff_scale, mass_scale):
    stiff_part, mass_part = diag_tables()
    product = stiff_scale * conduct * jnp.asarray(
        stiff_part, conduct.dtype
    ) + mass_scale * jnp.asarray(mass_part, conduct.dtype)
    return gather_elements(product)


def coarse_conduct(conduct):
    layers_z, rows_y, cols_x = conduct.shape
    shaped = conduct.reshape(layers_z // 2, 2, rows_y // 2, 2, cols_x // 2, 2)
    return jnp.sum(shaped, axis=(1, 3, 5)) * 0.125


def prolong_axis(coarse, which_axis):
    pieces = node_slices(coarse, which_axis)
    fine_parts = [
        pieces[0],
        0.375 * pieces[0] + 0.75 * pieces[1] - 0.125 * pieces[2],
        pieces[1],
        -0.125 * pieces[0] + 0.75 * pieces[1] + 0.375 * pieces[2],
    ]
    woven_nodes = jnp.stack(fine_parts, axis=which_axis + 1)
    node_shape = list(pieces[0].shape)
    node_shape[which_axis] = 4 * pieces[0].shape[which_axis]
    woven_nodes = woven_nodes.reshape(node_shape)
    length_here = coarse.shape[which_axis]
    tail_node = lax.slice_in_dim(coarse, length_here - 1, length_here, axis=which_axis)
    return jnp.concatenate([woven_nodes, tail_node], axis=which_axis)


def prolong_all(coarse):
    result = prolong_axis(coarse, 0)
    result = prolong_axis(result, 1)
    return prolong_axis(result, 2)


def restrict_axis(fine, which_axis):
    length_here = fine.shape[which_axis]
    elements = (length_here - 1) // 4
    quarters = [
        lax.slice_in_dim(fine, q, q + 4 * elements - 3, 4, axis=which_axis) for q in range(4)
    ]
    coarse_parts = [
        quarters[0] + 0.375 * quarters[1] - 0.125 * quarters[3],
        0.75 * quarters[1] + quarters[2] + 0.75 * quarters[3],
        -0.125 * quarters[1] + 0.375 * quarters[3],
    ]
    folded = fold_back(jnp.stack(coarse_parts, 0), which_axis + 1)
    tail_node = lax.slice_in_dim(fine, length_here - 1, length_here, axis=which_axis)
    return folded + pad_axis(tail_node, which_axis, 2 * elements, 0)


def restrict_all(fine):
    result = restrict_axis(fine, 0)
    result = restrict_axis(result, 1)
    return restrict_axis(result, 2)


def chebyshev(right_side, diagonal, operate, degree):
    centre = 0.5 * (upper_bound + lower_bound)
    half_width = 0.5 * (upper_bound - lower_bound)
    sharpness = centre / half_width
    factor = 1.0 / sharpness
    scaled = 1.0 / diagonal
    update = scaled * right_side * (1.0 / centre)
    solution = update
    for k in range(1, degree):
        residual = right_side - operate(solution)
        next_factor = 1.0 / (2.0 * sharpness - factor)
        update = next_factor * factor * update + 2.0 * next_factor / half_width * (
            scaled * residual
        )
        solution = solution + update
        factor = next_factor
    return solution


def merge_rims(extended, which_axis):
    length_here = extended.shape[which_axis]
    inner_part = lax.slice_in_dim(extended, 1, length_here - 1, axis=which_axis)
    below_rim = lax.slice_in_dim(extended, 0, 1, axis=which_axis)
    above_rim = lax.slice_in_dim(extended, length_here - 1, length_here, axis=which_axis)
    return (
        inner_part
        + pad_axis(below_rim, which_axis, 0, length_here - 3)
        + pad_axis(above_rim, which_axis, length_here - 3, 0)
    )


def merge_all(extended, axes_list):
    for which_axis in axes_list:
        extended = merge_rims(extended, which_axis)
    return extended


def faces_fine(stacked):
    extended = padded(stacked, (("gx", 3), ("gy", 2), ("gz", 1)), 1)
    return merge_all(extended, (1, 2, 3))


def coarse_sums(stacked):
    extended = padded(stacked, (("gx", 3), ("gy", 2), ("gz", 1)), 1)
    return merge_all(extended, (1, 2, 3))


def widened(stacked, sides, width):
    for axis, dim in sides:
        count = lax.axis_size(axis)
        length_here = stacked.shape[dim]
        head = lax.slice_in_dim(stacked, 0, width, axis=dim)
        tail = lax.slice_in_dim(stacked, length_here - width, length_here, axis=dim)
        below = lax.ppermute(tail, axis, [(i, (i + 1) % count) for i in range(count)])
        above = lax.ppermute(head, axis, [((i + 1) % count, i) for i in range(count)])
        stacked = jnp.concatenate(
            [
                lax.slice_in_dim(below, 0, width - 1, axis=dim),
                lax.slice_in_dim(below, width - 1, width, axis=dim)
                + lax.slice_in_dim(stacked, 0, 1, axis=dim),
                lax.slice_in_dim(stacked, 1, length_here - 1, axis=dim),
                lax.slice_in_dim(stacked, length_here - 1, length_here, axis=dim)
                + lax.slice_in_dim(above, 0, 1, axis=dim),
                lax.slice_in_dim(above, 1, width, axis=dim),
            ],
            axis=dim,
        )
    return stacked


def on_device(element_load, conductivity):
    load_full = pad_axis(element_load, 2, 0, 1)
    cond_nodes = lax.pad(
        conductivity, jnp.zeros((), conductivity.dtype), [(0, 2, 1), (0, 2, 1), (0, 2, 1)]
    )
    ring = 2
    wide = widened(
        jnp.stack([load_full, diag_local(conductivity, 1.0, reaction_rate), cond_nodes], 0),
        (("gx", 3), ("gy", 2), ("gz", 1)),
        ring + 1,
    )
    inner = wide[:, ring:-ring, ring:-ring, ring:-ring]
    right_side = inner[0]
    diagonal = inner[1]
    cells = conductivity.shape
    wide_x = wide.shape[3]
    order = np.concatenate([np.arange(0, wide_x, 2), np.arange(1, wide_x, 2)])
    chooser = np.zeros((wide_x, wide_x), np.float32)
    chooser[order, np.arange(wide_x)] = 1.0
    cond_even = jnp.einsum(
        "zyx,xk->zyk", wide[2], jnp.asarray(chooser), precision=lax.Precision.HIGHEST
    )
    cond_wide = cond_even[: 2 * cells[0] + 3 : 2, : 2 * cells[1] + 3 : 2, : cells[2] + 2]

    def operate_fine(node_field):
        return faces_fine(apply_local(node_field, conductivity, 1.0, reaction_rate)[None])[0]

    centre = 0.5 * (upper_bound + lower_bound)
    half_width = 0.5 * (upper_bound - lower_bound)
    sharpness = centre / half_width
    factor = 1.0 / sharpness
    scaled = 1.0 / diagonal
    update = scaled * right_side * (1.0 / centre)
    smooth = update
    first_wide = 1.0 / wide[1] * wide[0] * (1.0 / centre)
    applied_first = apply_local(first_wide, cond_wide, 1.0, reaction_rate)[
        ring:-ring, ring:-ring, ring:-ring
    ]
    for k in range(1, DEG1):
        if k == 1:
            residual = right_side - applied_first
        else:
            residual = right_side - operate_fine(smooth)
        next_factor = 1.0 / (2.0 * sharpness - factor)
        update = next_factor * factor * update + 2.0 * next_factor / half_width * (
            scaled * residual
        )
        smooth = smooth + update
        factor = next_factor
    partial_value = load_full - apply_local(smooth, conductivity, 1.0, reaction_rate)
    coarse_load = restrict_all(partial_value)
    coarse_cond = coarse_conduct(conductivity)
    coarse_mass = 8.0 * reaction_rate
    coarse_diag = diag_local(coarse_cond, 2.0, coarse_mass)
    coarse_both = coarse_sums(jnp.stack([coarse_load, coarse_diag], 0))

    def operate_coarse(node_field):
        return coarse_sums(apply_local(node_field, coarse_cond, 2.0, coarse_mass)[None])[0]

    correction = chebyshev(coarse_both[0], coarse_both[1], operate_coarse, DEG2)
    corrected = smooth + prolong_all(correction)
    return corrected[:, :, : corrected.shape[2] - 1]


def solution(mesh):
    in_specs = (P("gz", "gy", "gx"), P("gz", "gy", "gx"))
    out_specs = P("gz", "gy", "gx")
    return jax.shard_map(
        on_device, mesh=mesh, in_specs=in_specs, out_specs=out_specs, check_vma=False
    )
```
